768 devices in a mesh: row: 48 (over z_lo, x, core), col: 16 (over y, z_hi).
Axes of the slice: x: 4, y: 8, z: 12 (z_hi: 2, z_lo: 6; z = z_hi * 6 + z_lo), core: 2. Of those that a mesh axis runs over, the one named last changes fastest.
Arguments:
- matrix: float32 [61440, 6144], P('row', 'col'), may hold values from -1 to 96, as said below
Outputs:
- stepped: float32 [61440, 6144], P('row', 'col')
The draws below stay inside these ranges and needn't reach their ends.
Inputs may be any that keep to these rules, and one draw needn't show every extreme that they name: `matrix`: entries where global row equals global column lie in 64 to 96; all other entries lie in -1 to 1, so the symmetrized first diagonal tile is positive definite.
All inputs are finite; a program needn't handle non-finite values.
Results may differ from the reference program's by a relative error of at most 0.0003.
Values sent between devices are 32-bit elements; how exact they have to be, the bound alone decides.
No kernel may reach another device: no remote copies, remote signals or barrier semaphores. Data moves between devices by JAX's collectives and lax.ppermute only.
A program may use at most 32 MiB of HBM per device.

```python
import jax
import jax.numpy as jnp
from jax import lax

N = 61440
B = 64
PROWS = 48
PCOLS = 16
W = 6144


def draw_matrix(key, part):
    rows_dev = N // PROWS
    cols_dev = W // PCOLS
    srow = jnp.arange(N, dtype=jnp.int32)
    local = srow % rows_dev
    global_rows = (local // B * PROWS + srow // rows_dev) * B + local % B
    scol = jnp.arange(W, dtype=jnp.int32)
    clocal = scol % cols_dev
    global_cols = (clocal // B * PCOLS + scol // cols_dev) * B + clocal % B
    key_off = jax.random.fold_in(key, 11)
    key_diag = jax.random.fold_in(key, 23)
    offdiag = jax.random.uniform(key_off, (N, W), jnp.float32, -1.0, 1.0)
    diagonal = jax.random.uniform(key_diag, (N, W), jnp.float32, 64.0, 96.0)
    same = global_rows[:, None] == global_cols[None, :]
    return jnp.where(same, diagonal, offdiag)


def setup_inputs(seed: int = 0) -> dict:
    streams_of = jax.random.split(jax.random.key(seed), 2)
    matrix = draw_matrix(jax.random.fold_in(streams_of[1], 71), 0)
    return {"matrix": matrix}


def reference(matrix):
    rows_dev = N // PROWS
    cols_dev = W // PCOLS
    srow = jnp.arange(N, dtype=jnp.int32)
    owner = srow // rows_dev
    local = srow % rows_dev
    global_rows = (local // B * PROWS + owner) * B + local % B
    scol = jnp.arange(W, dtype=jnp.int32)
    cowner = scol // cols_dev
    clocal = scol % cols_dev
    global_cols = (clocal // B * PCOLS + cowner) * B + clocal % B
    tile = matrix[:B, :B]
    corner = (tile + tile.T) / 2.0
    factor = jnp.linalg.cholesky(corner)
    solved = lax.linalg.triangular_solve(factor, matrix[:, :B].T, left_side=True, lower=True)
    panel_factor = solved.T
    panel_factor = panel_factor.at[:B].set(factor)
    tiles = global_cols // B
    where_row = tiles % PROWS * rows_dev + tiles // PROWS * B + global_cols % B
    column_factor = jnp.take(panel_factor, where_row.astype(jnp.int32), axis=0)
    blocks = matrix.reshape(PROWS, rows_dev, W)
    lower_blocks = panel_factor.reshape(PROWS, rows_dev, B)
    grow_blocks = global_rows.reshape(PROWS, rows_dev)

    def update_block(items):
        block, lower, grow = items
        change = jnp.dot(lower.astype(jnp.float32), column_factor.T.astype(jnp.float32), precision=lax.Precision.HIGHEST, preferred_element_type=jnp.float32)
        return jnp.where((grow < B)[:, None], block, block - change)
    stepped = lax.map(update_block, (blocks, lower_blocks, grow_blocks)).reshape(N, W)
    stepped = stepped.at[:, :B].set(panel_factor)
    return stepped
```

```python
import jax
import jax.numpy as jnp
from jax import lax
from jax.sharding import PartitionSpec as P

B = 64
RADIX = 2


def tree_broadcast(x, axes, size, index_of, member, radix=RADIX):
    have = 1
    while have < size:
        fresh = x
        for c in range(1, radix):
            lo = c * have
            if lo >= size:
                break
            pairs = []
            for src in index_of(None):
                for m in range(have):
                    if m + lo < size:
                        pairs.append((src(m), src(m + lo)))
            got = lax.ppermute(x, axes, pairs)
            take = jnp.logical_and(member >= lo, member < lo + have)
            fresh = jnp.where(take, got, fresh)
        x = fresh
        have *= radix
    return x


def shards(matrix):
    rows_dev, cols_dev = matrix.shape
    n_row = lax.axis_size("row")
    n_col = lax.axis_size("col")
    row_id = lax.axis_index("row")
    col_id = lax.axis_index("col")
    n_src = n_row // n_col
    window_cols = cols_dev * n_col // n_row

    panel_t = matrix[:, :B].T

    def col_groups(_):
        return [lambda m, r=r: r * n_col + m for r in range(n_row)]

    panel_t = tree_broadcast(panel_t, ("row", "col"), n_col, col_groups, col_id)

    head = panel_t[:, :window_cols]
    rel = (row_id - col_id) % n_row
    my_j = rel // n_col
    is_src = rel % n_col == 0
    pieces = [head]
    for c in range(1, n_src):
        pairs = []
        for q in range(n_col):
            for j in range(n_src):
                a = q + n_col * j
                b = q + n_col * ((j + c) % n_src)
                pairs.append((a * n_col + q, b * n_col + q))
        pieces.append(lax.ppermute(head, ("row", "col"), pairs))
    corner_t = panel_t[:, :B]
    got_corner = jnp.zeros_like(corner_t)
    for j in range(n_src):
        pairs = []
        for q in range(n_col):
            b = q + n_col * j
            if b != 0:
                pairs.append((0 * n_col + q, b * n_col + q))
        got_corner = got_corner + lax.ppermute(corner_t, ("row", "col"), pairs)
    corner_t = jnp.where(row_id == 0, corner_t, got_corner)
    ordered = []
    for jj in range(n_src):
        pick = pieces[0]
        for c in range(1, n_src):
            pick = jnp.where((my_j - jj) % n_src == c, pieces[c], pick)
        ordered.append(pick)
    packet = jnp.concatenate(ordered + [corner_t], axis=1)
    packet = jnp.where(is_src, packet, jnp.zeros_like(packet))

    def row_groups(_):
        out = []
        for q in range(n_col):
            for j in range(n_src):
                base = q + n_col * j
                out.append(lambda m, base=base, q=q: ((base + m) % n_row) * n_col + q)
        return out

    packet = tree_broadcast(packet, ("row", "col"), n_col, row_groups, rel % n_col)

    corner_t = packet[:, n_src * window_cols:]
    corner = (corner_t + corner_t.T) / 2.0
    factor = jnp.linalg.cholesky(corner)

    tiles = []
    for k in range(cols_dev // B):
        j = k % n_src
        lt = k // n_src
        tiles.append(packet[:, j * window_cols + lt * B: j * window_cols + (lt + 1) * B])
    window_t = jnp.concatenate(tiles, axis=1)

    both = jnp.concatenate([panel_t, window_t], axis=1)
    solved = lax.linalg.triangular_solve(factor, both, left_side=True, lower=True)
    lower_t = solved[:, :rows_dev]
    lower_t = jnp.concatenate(
        [jnp.where(row_id == 0, factor.T, lower_t[:, :B]), lower_t[:, B:]], axis=1
    )
    col_t = solved[:, rows_dev:]
    col_t = jnp.concatenate(
        [jnp.where(col_id == 0, factor.T, col_t[:, :B]), col_t[:, B:]], axis=1
    )
    change = lax.dot_general(
        lower_t,
        col_t,
        (((0,), (0,)), ((), ())),
        precision=lax.Precision.HIGHEST,
        preferred_element_type=jnp.float32,
    )
    local_rows = jnp.arange(rows_dev, dtype=jnp.int32)
    keep_rows = jnp.logical_and(row_id == 0, local_rows < B)
    stepped = jnp.where(keep_rows[:, None], matrix, matrix - change)
    first_cols = jnp.where(col_id == 0, lower_t.T, stepped[:, :B])
    return jnp.concatenate([first_cols, stepped[:, B:]], axis=1)


def solution(mesh):
    placed = (P("row", "col"),)
    return jax.shard_map(
        shards, mesh=mesh, in_specs=placed, out_specs=P("row", "col"), check_vma=False
    )
```

```python
import jax
import jax.numpy as jnp
from jax import lax
from jax.sharding import PartitionSpec as P

B = 64
RADIX = 4


def tree_broadcast(x, axes, size, index_of, member, radix=RADIX):
    have = 1
    while have < size:
        fresh = x
        for c in range(1, radix):
            lo = c * have
            if lo >= size:
                break
            pairs = []
            for src in index_of(None):
                for m in range(have):
                    if m + lo < size:
                        pairs.append((src(m), src(m + lo)))
            got = lax.ppermute(x, axes, pairs)
            take = jnp.logical_and(member >= lo, member < lo + have)
            fresh = jnp.where(take, got, fresh)
        x = fresh
        have *= radix
    return x


def shards(matrix):
    rows_dev, cols_dev = matrix.shape
    n_row = lax.axis_size("row")
    n_col = lax.axis_size("col")
    row_id = lax.axis_index("row")
    col_id = lax.axis_index("col")
    n_src = n_row // n_col
    window_cols = cols_dev * n_col // n_row

    panel_t = matrix[:, :B].T

    def col_groups(_):
        return [lambda m, r=r: r * n_col + m for r in range(n_row)]

    panel_t = tree_broadcast(panel_t, ("row", "col"), n_col, col_groups, col_id)

    head = panel_t[:, :window_cols]
    rel = (row_id - col_id) % n_row
    my_j = rel // n_col
    is_src = rel % n_col == 0
    pieces = [head]
    for c in range(1, n_src):
        pairs = []
        for q in range(n_col):
            for j in range(n_src):
                a = q + n_col * j
                b = q + n_col * ((j + c) % n_src)
                pairs.append((a * n_col + q, b * n_col + q))
        pieces.append(lax.ppermute(head, ("row", "col"), pairs))
    corner_t = panel_t[:, :B]
    got_corner = jnp.zeros_like(corner_t)
    for j in range(n_src):
        pairs = []
        for q in range(n_col):
            b = q + n_col * j
            if b != 0:
                pairs.append((0 * n_col + q, b * n_col + q))
        got_corner = got_corner + lax.ppermute(corner_t, ("row", "col"), pairs)
    corner_t = jnp.where(row_id == 0, corner_t, got_corner)
    ordered = []
    for jj in range(n_src):
        pick = pieces[0]
        for c in range(1, n_src):
            pick = jnp.where((my_j - jj) % n_src == c, pieces[c], pick)
        ordered.append(pick)
    packet = jnp.concatenate(ordered + [corner_t], axis=1)
    packet = jnp.where(is_src, packet, jnp.zeros_like(packet))

    def row_groups(_):
        out = []
        for q in range(n_col):
            for j in range(n_src):
                base = q + n_col * j
                out.append(lambda m, base=base, q=q: ((base + m) % n_row) * n_col + q)
        return out

    packet = tree_broadcast(packet, ("row", "col"), n_col, row_groups, rel % n_col)

    corner_t = packet[:, n_src * window_cols:]
    corner = (corner_t + corner_t.T) / 2.0
    factor = jnp.linalg.cholesky(corner)

    tiles = []
    for k in range(cols_dev // B):
        j = k % n_src
        lt = k // n_src
        tiles.append(packet[:, j * window_cols + lt * B: j * window_cols + (lt + 1) * B])
    window_t = jnp.concatenate(tiles, axis=1)

    both = jnp.concatenate([panel_t, window_t], axis=1)
    solved = lax.linalg.triangular_solve(factor, both, left_side=True, lower=True)
    lower_t = solved[:, :rows_dev]
    lower_t = jnp.concatenate(
        [jnp.where(row_id == 0, factor.T, lower_t[:, :B]), lower_t[:, B:]], axis=1
    )
    col_t = solved[:, rows_dev:]
    col_t = jnp.concatenate(
        [jnp.where(col_id == 0, factor.T, col_t[:, :B]), col_t[:, B:]], axis=1
    )
    change = lax.dot_general(
        lower_t,
        col_t,
        (((0,), (0,)), ((), ())),
        precision=lax.Precision.HIGHEST,
        preferred_element_type=jnp.float32,
    )
    local_rows = jnp.arange(rows_dev, dtype=jnp.int32)
    keep_rows = jnp.logical_and(row_id == 0, local_rows < B)
    stepped = jnp.where(keep_rows[:, None], matrix, matrix - change)
    first_cols = jnp.where(col_id == 0, lower_t.T, stepped[:, :B])
    return jnp.concatenate([first_cols, stepped[:, B:]], axis=1)


def solution(mesh):
    placed = (P("row", "col"),)
    return jax.shard_map(
        shards, mesh=mesh, in_specs=placed, out_specs=P("row", "col"), check_vma=False
    )
```

```python
import jax
import jax.numpy as jnp
from jax import lax
from jax.sharding import PartitionSpec as P

B = 64
RADIX = 2


def tree_broadcast(x, axes, size, index_of, member, radix=RADIX):
    have = 1
    while have < size:
        fresh = x
        for c in range(1, radix):
            lo = c * have
            if lo >= size:
                break
            pairs = []
            for src in index_of(None):
                for m in range(have):
                    if m + lo < size:
                        pairs.append((src(m), src(m + lo)))
            got = lax.ppermute(x, axes, pairs)
            take = jnp.logical_and(member >= lo, member < lo + have)
            fresh = jnp.where(take, got, fresh)
        x = fresh
        have *= radix
    return x


def shards(matrix):
    rows_dev, cols_dev = matrix.shape
    n_row = lax.axis_size("row")
    n_col = lax.axis_size("col")
    row_id = lax.axis_index("row")
    col_id = lax.axis_index("col")
    n_src = n_row // n_col
    window_cols = cols_dev * n_col // n_row

    panel_t = matrix[:, :B].T
    head = panel_t[:, :window_cols]

    def col0_group(_):
        return [lambda m: m * n_col]

    corner_t = tree_broadcast(panel_t[:, :B], ("row", "col"), n_row, col0_group, row_id, radix=4)

    def col_groups(_):
        return [lambda m, r=r: r * n_col + m for r in range(n_row)]

    with_corner = jnp.concatenate([panel_t, corner_t], axis=1)
    with_corner = tree_broadcast(with_corner, ("row", "col"), n_col, col_groups, col_id)
    panel_t = with_corner[:, :rows_dev]
    corner_t = with_corner[:, rows_dev:]

    pairs = [(r * n_col, r * n_col + r % n_col) for r in range(n_row) if r % n_col]
    got = lax.ppermute(head, ("row", "col"), pairs)
    head = jnp.where(col_id == 0, head, got)
    rel = (row_id - col_id) % n_row
    my_j = rel // n_col
    is_src = rel % n_col == 0
    pieces = [head]
    for c in range(1, n_src):
        pairs = []
        for q in range(n_col):
            for j in range(n_src):
                a = q + n_col * j
                b = q + n_col * ((j + c) % n_src)
                pairs.append((a * n_col + q, b * n_col + q))
        pieces.append(lax.ppermute(head, ("row", "col"), pairs))
    ordered = []
    for jj in range(n_src):
        pick = pieces[0]
        for c in range(1, n_src):
            pick = jnp.where((my_j - jj) % n_src == c, pieces[c], pick)
        ordered.append(pick)
    packet = jnp.concatenate(ordered, axis=1)
    packet = jnp.where(is_src, packet, jnp.zeros_like(packet))

    def row_groups(_):
        out = []
        for q in range(n_col):
            for j in range(n_src):
                base = q + n_col * j
                out.append(lambda m, base=base, q=q: ((base + m) % n_row) * n_col + q)
        return out

    packet = tree_broadcast(packet, ("row", "col"), n_col, row_groups, rel % n_col)

    corner = (corner_t + corner_t.T) / 2.0
    factor = jnp.linalg.cholesky(corner)

    tiles = []
    for k in range(cols_dev // B):
        j = k % n_src
        lt = k // n_src
        tiles.append(packet[:, j * window_cols + lt * B: j * window_cols + (lt + 1) * B])
    window_t = jnp.concatenate(tiles, axis=1)

    both = jnp.concatenate([panel_t, window_t], axis=1)
    solved = lax.linalg.triangular_solve(factor, both, left_side=True, lower=True)
    lower_t = solved[:, :rows_dev]
    lower_t = jnp.concatenate(
        [jnp.where(row_id == 0, factor.T, lower_t[:, :B]), lower_t[:, B:]], axis=1
    )
    col_t = solved[:, rows_dev:]
    col_t = jnp.concatenate(
        [jnp.where(col_id == 0, factor.T, col_t[:, :B]), col_t[:, B:]], axis=1
    )
    change = lax.dot_general(
        lower_t,
        col_t,
        (((0,), (0,)), ((), ())),
        precision=lax.Precision.HIGHEST,
        preferred_element_type=jnp.float32,
    )
    local_rows = jnp.arange(rows_dev, dtype=jnp.int32)
    keep_rows = jnp.logical_and(row_id == 0, local_rows < B)
    stepped = jnp.where(keep_rows[:, None], matrix, matrix - change)
    first_cols = jnp.where(col_id == 0, lower_t.T, stepped[:, :B])
    return jnp.concatenate([first_cols, stepped[:, B:]], axis=1)


def solution(mesh):
    placed = (P("row", "col"),)
    return jax.shard_map(
        shards, mesh=mesh, in_specs=placed, out_specs=P("row", "col"), check_vma=False
    )
```

```python
import jax
import jax.numpy as jnp
from jax import lax
from jax.sharding import PartitionSpec as P

B = 64
RADIX = 2


def tree_broadcast(x, axes, size, index_of, member, radix=RADIX):
    have = 1
    while have < size:
        x = tree_round(x, axes, size, index_of, member, have, radix)
        have *= radix
    return x


def tree_round(x, axes, size, index_of, member, have, radix=RADIX):
    if True:
        fresh = x
        for c in range(1, radix):
            lo = c * have
            if lo >= size:
                break
            pairs = []
            for src in index_of(None):
                for m in range(have):
                    if m + lo < size:
                        pairs.append((src(m), src(m + lo)))
            got = lax.ppermute(x, axes, pairs)
            take = jnp.logical_and(member >= lo, member < lo + have)
            fresh = jnp.where(take, got, fresh)
    return fresh


def shards(matrix):
    rows_dev, cols_dev = matrix.shape
    n_row = lax.axis_size("row")
    n_col = lax.axis_size("col")
    row_id = lax.axis_index("row")
    col_id = lax.axis_index("col")
    n_src = n_row // n_col
    window_cols = cols_dev * n_col // n_row

    panel_t = matrix[:, :B].T
    head = panel_t[:, :window_cols]

    def col_groups(_):
        return [lambda m, r=r: r * n_col + m for r in range(n_row)]

    full_t = tree_round(panel_t, ("row", "col"), n_col, col_groups, col_id, 1)
    full_t, head, corner_in = lax.optimization_barrier((full_t, head, panel_t[:, :B]))

    to_owner = [(r * n_col, r * n_col + r % n_col) for r in range(n_row) if r % n_col]
    got = lax.ppermute(head, ("row", "col"), to_owner)
    head = jnp.where(col_id == 0, head, got)
    rel = (row_id - col_id) % n_row
    my_j = rel // n_col
    is_src = rel % n_col == 0
    pieces = [head]
    for c in range(1, n_src):
        pairs = []
        for q in range(n_col):
            for j in range(n_src):
                a = q + n_col * j
                b = q + n_col * ((j + c) % n_src)
                pairs.append((a * n_col + q, b * n_col + q))
        pieces.append(lax.ppermute(head, ("row", "col"), pairs))
    ordered = []
    for jj in range(n_src):
        pick = pieces[0]
        for c in range(1, n_src):
            pick = jnp.where((my_j - jj) % n_src == c, pieces[c], pick)
        ordered.append(pick)

    def col0_group(_):
        return [lambda m: m * n_col]

    corner_t = tree_broadcast(corner_in, ("row", "col"), n_row, col0_group, row_id, radix=4)
    full_t = tree_round(full_t, ("row", "col"), n_col, col_groups, col_id, 2)
    full_t, corner_t = lax.optimization_barrier((full_t, corner_t))
    corner = (corner_t + corner_t.T) / 2.0
    factor = jnp.linalg.cholesky(corner)
    inverse = lax.linalg.triangular_solve(
        factor, jnp.eye(B, dtype=factor.dtype), left_side=True, lower=True
    )
    fpack = jnp.concatenate([factor.T, inverse], axis=1)
    full_t = tree_round(full_t, ("row", "col"), n_col, col_groups, col_id, 4)
    full_t, fpack = lax.optimization_barrier((full_t, fpack))
    have = 8
    while have < n_col:
        full_t = tree_round(full_t, ("row", "col"), n_col, col_groups, col_id, have)
        have *= 2
    got = lax.ppermute(fpack, ("row", "col"), to_owner)
    fpack = jnp.where(col_id == 0, fpack, got)

    packet = jnp.concatenate(ordered + [fpack], axis=1)
    packet = jnp.where(is_src, packet, jnp.zeros_like(packet))

    def row_groups(_):
        out = []
        for q in range(n_col):
            for j in range(n_src):
                base = q + n_col * j
                out.append(lambda m, base=base, q=q: ((base + m) % n_row) * n_col + q)
        return out

    packet = tree_broadcast(packet, ("row", "col"), n_col, row_groups, rel % n_col)
    factor_t = packet[:, n_src * window_cols: n_src * window_cols + B]
    inverse = packet[:, n_src * window_cols + B: n_src * window_cols + 2 * B]

    tiles = []
    for k in range(cols_dev // B):
        j = k % n_src
        lt = k // n_src
        tiles.append(packet[:, j * window_cols + lt * B: j * window_cols + (lt + 1) * B])
    window_t = jnp.concatenate(tiles, axis=1)

    def apply(x):
        return lax.dot(inverse, x, precision=lax.Precision.HIGHEST,
                       preferred_element_type=jnp.float32)

    lower_t = apply(full_t)
    lower_t = jnp.concatenate(
        [jnp.where(row_id == 0, factor_t, lower_t[:, :B]), lower_t[:, B:]], axis=1
    )
    col_t = apply(window_t)
    col_t = jnp.concatenate(
        [jnp.where(col_id == 0, factor_t, col_t[:, :B]), col_t[:, B:]], axis=1
    )
    change = lax.dot_general(
        lower_t,
        col_t,
        (((0,), (0,)), ((), ())),
        precision=lax.Precision.HIGHEST,
        preferred_element_type=jnp.float32,
    )
    local_rows = jnp.arange(rows_dev, dtype=jnp.int32)
    keep_rows = jnp.logical_and(row_id == 0, local_rows < B)
    stepped = jnp.where(keep_rows[:, None], matrix, matrix - change)
    first_cols = jnp.where(col_id == 0, lower_t.T, stepped[:, :B])
    return jnp.concatenate([first_cols, stepped[:, B:]], axis=1)


def solution(mesh):
    placed = (P("row", "col"),)
    return jax.shard_map(
        shards, mesh=mesh, in_specs=placed, out_specs=P("row", "col"), check_vma=False
    )
```

```python
import jax
import jax.numpy as jnp
from jax import lax
from jax.sharding import PartitionSpec as P

B = 64
RADIX = 2


def tree_broadcast(x, axes, size, index_of, member, radix=RADIX):
    have = 1
    while have < size:
        x = tree_round(x, axes, size, index_of, member, have, radix)
        have *= radix
    return x


def tree_round(x, axes, size, index_of, member, have, radix=RADIX):
    if True:
        fresh = x
        for c in range(1, radix):
            lo = c * have
            if lo >= size:
                break
            pairs = []
            for src in index_of(None):
                for m in range(have):
                    if m + lo < size:
                        pairs.append((src(m), src(m + lo)))
            got = lax.ppermute(x, axes, pairs)
            take = jnp.logical_and(member >= lo, member < lo + have)
            fresh = jnp.where(take, got, fresh)
    return fresh


def shards(matrix):
    rows_dev, cols_dev = matrix.shape
    n_row = lax.axis_size("row")
    n_col = lax.axis_size("col")
    row_id = lax.axis_index("row")
    col_id = lax.axis_index("col")
    n_src = n_row // n_col
    window_cols = cols_dev * n_col // n_row

    panel_t = matrix[:, :B].T
    head = panel_t[:, :window_cols]

    def col0_group(_):
        return [lambda m: m * n_col]

    corner_t = tree_broadcast(panel_t[:, :B], ("row", "col"), n_row, col0_group, row_id, radix=4)
    panel_t, head, corner_t = lax.optimization_barrier((panel_t, head, corner_t))

    def col_groups(_):
        return [lambda m, r=r: r * n_col + m for r in range(n_row)]

    def panel_round(x, have):
        return tree_round(x, ("row", "col"), n_col, col_groups, col_id, have)

    panel_t = panel_round(panel_t, 1)

    pairs = [(r * n_col, r * n_col + r % n_col) for r in range(n_row) if r % n_col]
    first = jnp.concatenate([head, corner_t], axis=1)
    got = lax.ppermute(first, ("row", "col"), pairs)
    first = jnp.where(col_id == 0, first, got)
    panel_t, first = lax.optimization_barrier((panel_t, first))
    panel_t = panel_round(panel_t, 2)
    head = first[:, :window_cols]
    corner_t = first[:, window_cols:]
    rel = (row_id - col_id) % n_row
    my_j = rel // n_col
    is_src = rel % n_col == 0
    pieces = [head]
    for c in range(1, n_src):
        pairs = []
        for q in range(n_col):
            for j in range(n_src):
                a = q + n_col * j
                b = q + n_col * ((j + c) % n_src)
                pairs.append((a * n_col + q, b * n_col + q))
        pieces.append(lax.ppermute(head, ("row", "col"), pairs))
    ordered = []
    for jj in range(n_src):
        pick = pieces[0]
        for c in range(1, n_src):
            pick = jnp.where((my_j - jj) % n_src == c, pieces[c], pick)
        ordered.append(pick)
    packet = jnp.concatenate(ordered + [corner_t], axis=1)
    packet = jnp.where(is_src, packet, jnp.zeros_like(packet))
    panel_t, packet = lax.optimization_barrier((panel_t, packet))

    def row_groups(_):
        out = []
        for q in range(n_col):
            for j in range(n_src):
                base = q + n_col * j
                out.append(lambda m, base=base, q=q: ((base + m) % n_row) * n_col + q)
        return out

    have = 1
    while have < n_col:
        packet = tree_round(packet, ("row", "col"), n_col, row_groups, rel % n_col, have)
        if 4 * have < n_col:
            panel_t = panel_round(panel_t, 4 * have)
            panel_t, packet = lax.optimization_barrier((panel_t, packet))
        have *= 2

    corner_t = packet[:, n_src * window_cols:]
    corner = (corner_t + corner_t.T) / 2.0
    factor = jnp.linalg.cholesky(corner)
    inverse = lax.linalg.triangular_solve(
        factor, jnp.eye(B, dtype=factor.dtype), left_side=True, lower=True
    )

    tiles = []
    for k in range(cols_dev // B):
        j = k % n_src
        lt = k // n_src
        tiles.append(packet[:, j * window_cols + lt * B: j * window_cols + (lt + 1) * B])
    window_t = jnp.concatenate(tiles, axis=1)

    def apply(x):
        return lax.dot(inverse, x, precision=lax.Precision.HIGHEST,
                       preferred_element_type=jnp.float32)

    col_t = apply(window_t)
    col_t = jnp.concatenate(
        [jnp.where(col_id == 0, factor.T, col_t[:, :B]), col_t[:, B:]], axis=1
    )
    lower_t = apply(panel_t)
    lower_t = jnp.concatenate(
        [jnp.where(row_id == 0, factor.T, lower_t[:, :B]), lower_t[:, B:]], axis=1
    )
    change = lax.dot_general(
        lower_t,
        col_t,
        (((0,), (0,)), ((), ())),
        precision=lax.Precision.HIGHEST,
        preferred_element_type=jnp.float32,
    )
    local_rows = jnp.arange(rows_dev, dtype=jnp.int32)
    keep_rows = jnp.logical_and(row_id == 0, local_rows < B)
    stepped = jnp.where(keep_rows[:, None], matrix, matrix - change)
    first_cols = jnp.where(col_id == 0, lower_t.T, stepped[:, :B])
    return jnp.concatenate([first_cols, stepped[:, B:]], axis=1)


def solution(mesh):
    placed = (P("row", "col"),)
    return jax.shard_map(
        shards, mesh=mesh, in_specs=placed, out_specs=P("row", "col"), check_vma=False
    )
```

```python
import jax
import jax.numpy as jnp
from jax import lax
from jax.sharding import PartitionSpec as P

B = 64
RADIX = 2


def tree_broadcast(x, axes, size, index_of, member, radix=RADIX):
    have = 1
    while have < size:
        fresh = x
        for c in range(1, radix):
            lo = c * have
            if lo >= size:
                break
            pairs = []
            for src in index_of(None):
                for m in range(have):
                    if m + lo < size:
                        pairs.append((src(m), src(m + lo)))
            got = lax.ppermute(x, axes, pairs)
            take = jnp.logical_and(member >= lo, member < lo + have)
            fresh = jnp.where(take, got, fresh)
        x = fresh
        have *= radix
    return x


def shards(matrix):
    rows_dev, cols_dev = matrix.shape
    n_row = lax.axis_size("row")
    n_col = lax.axis_size("col")
    row_id = lax.axis_index("row")
    col_id = lax.axis_index("col")
    n_src = n_row // n_col
    window_cols = cols_dev * n_col // n_row

    panel_t = matrix[:, :B].T
    head = panel_t[:, :window_cols]

    def col0_group(_):
        return [lambda m: m * n_col]

    corner_t = tree_broadcast(panel_t[:, :B], ("row", "col"), n_row, col0_group, row_id, radix=4)

    def col_groups(_):
        return [lambda m, r=r: r * n_col + m for r in range(n_row)]

    with_corner = jnp.concatenate([panel_t, corner_t], axis=1)
    with_corner = tree_broadcast(with_corner, ("row", "col"), n_col, col_groups, col_id)
    panel_t = with_corner[:, :rows_dev]
    corner_t = with_corner[:, rows_dev:]

    rel = (row_id - col_id) % n_row
    my_j = rel // n_col
    is_src = rel % n_col == 0
    pieces = []
    for c in range(n_src):
        pairs = []
        for r in range(n_row):
            q = r % n_col
            if c or q:
                pairs.append((r * n_col, ((r + n_col * c) % n_row) * n_col + q))
        got = lax.ppermute(head, ("row", "col"), pairs)
        if c == 0:
            got = jnp.where(col_id == 0, head, got)
        pieces.append(got)
    ordered = []
    for jj in range(n_src):
        pick = pieces[0]
        for c in range(1, n_src):
            pick = jnp.where((my_j - jj) % n_src == c, pieces[c], pick)
        ordered.append(pick)
    packet = jnp.concatenate(ordered, axis=1)
    packet = jnp.where(is_src, packet, jnp.zeros_like(packet))

    def row_groups(_):
        out = []
        for q in range(n_col):
            for j in range(n_src):
                base = q + n_col * j
                out.append(lambda m, base=base, q=q: ((base + m) % n_row) * n_col + q)
        return out

    packet = tree_broadcast(packet, ("row", "col"), n_col, row_groups, rel % n_col)

    corner = (corner_t + corner_t.T) / 2.0
    factor = jnp.linalg.cholesky(corner)

    tiles = []
    for k in range(cols_dev // B):
        j = k % n_src
        lt = k // n_src
        tiles.append(packet[:, j * window_cols + lt * B: j * window_cols + (lt + 1) * B])
    window_t = jnp.concatenate(tiles, axis=1)

    both = jnp.concatenate([panel_t, window_t], axis=1)
    solved = lax.linalg.triangular_solve(factor, both, left_side=True, lower=True)
    lower_t = solved[:, :rows_dev]
    lower_t = jnp.concatenate(
        [jnp.where(row_id == 0, factor.T, lower_t[:, :B]), lower_t[:, B:]], axis=1
    )
    col_t = solved[:, rows_dev:]
    col_t = jnp.concatenate(
        [jnp.where(col_id == 0, factor.T, col_t[:, :B]), col_t[:, B:]], axis=1
    )
    change = lax.dot_general(
        lower_t,
        col_t,
        (((0,), (0,)), ((), ())),
        precision=lax.Precision.HIGHEST,
        preferred_element_type=jnp.float32,
    )
    local_rows = jnp.arange(rows_dev, dtype=jnp.int32)
    keep_rows = jnp.logical_and(row_id == 0, local_rows < B)
    stepped = jnp.where(keep_rows[:, None], matrix, matrix - change)
    first_cols = jnp.where(col_id == 0, lower_t.T, stepped[:, :B])
    return jnp.concatenate([first_cols, stepped[:, B:]], axis=1)


def solution(mesh):
    placed = (P("row", "col"),)
    return jax.shard_map(
        shards, mesh=mesh, in_specs=placed, out_specs=P("row", "col"), check_vma=False
    )
```

```python
import jax
import jax.numpy as jnp
from jax import lax
from jax.sharding import PartitionSpec as P

B = 64
RADIX = 2


def tree_broadcast(x, axes, size, index_of, member, radix=RADIX, have=1):
    while have < size:
        fresh = x
        for c in range(1, radix):
            lo = c * have
            if lo >= size:
                break
            pairs = []
            for src in index_of(None):
                for m in range(have):
                    if m + lo < size:
                        pairs.append((src(m), src(m + lo)))
            got = lax.ppermute(x, axes, pairs)
            take = jnp.logical_and(member >= lo, member < lo + have)
            fresh = jnp.where(take, got, fresh)
        x = fresh
        have *= radix
    return x


def shards(matrix):
    rows_dev, cols_dev = matrix.shape
    n_row = lax.axis_size("row")
    n_col = lax.axis_size("col")
    row_id = lax.axis_index("row")
    col_id = lax.axis_index("col")
    n_src = n_row // n_col
    window_cols = cols_dev * n_col // n_row

    panel_t = matrix[:, :B].T
    head = panel_t[:, :window_cols]

    def col0_group(_):
        return [lambda m: m * n_col]

    corner_t = tree_broadcast(panel_t[:, :B], ("row", "col"), n_row, col0_group, row_id, radix=4)

    def col_groups(_):
        return [lambda m, r=r: r * n_col + m for r in range(n_row)]

    panel_t, corner_t = lax.optimization_barrier((panel_t, corner_t))
    panel_t = tree_broadcast(panel_t, ("row", "col"), 2, col_groups, col_id, radix=2, have=1)

    rel = (row_id - col_id) % n_row
    my_j = rel // n_col
    is_src = rel % n_col == 0
    first = jnp.concatenate([head, corner_t], axis=1)
    pieces = []
    for c in range(n_src):
        pairs = []
        for r in range(n_row):
            q = r % n_col
            if c or q:
                pairs.append((r * n_col, ((r + n_col * c) % n_row) * n_col + q))
        got = lax.ppermute(first, ("row", "col"), pairs)
        if c == 0:
            got = jnp.where(col_id == 0, first, got)
        pieces.append(got)
    panel_t, pieces = lax.optimization_barrier((panel_t, pieces))
    panel_t = tree_broadcast(panel_t, ("row", "col"), n_col, col_groups, col_id, radix=2, have=2)
    corner_t = pieces[0][:, window_cols:]
    pieces = [p[:, :window_cols] for p in pieces]
    ordered = []
    for jj in range(n_src):
        pick = pieces[0]
        for c in range(1, n_src):
            pick = jnp.where((my_j - jj) % n_src == c, pieces[c], pick)
        ordered.append(pick)
    packet = jnp.concatenate(ordered + [corner_t], axis=1)
    packet = jnp.where(is_src, packet, jnp.zeros_like(packet))

    def row_groups(_):
        out = []
        for q in range(n_col):
            for j in range(n_src):
                base = q + n_col * j
                out.append(lambda m, base=base, q=q: ((base + m) % n_row) * n_col + q)
        return out

    packet = tree_broadcast(packet, ("row", "col"), n_col, row_groups, rel % n_col)

    corner_t = packet[:, n_src * window_cols:]
    corner = (corner_t + corner_t.T) / 2.0
    factor = jnp.linalg.cholesky(corner)
    inverse = lax.linalg.triangular_solve(
        factor, jnp.eye(B, dtype=factor.dtype), left_side=True, lower=True
    )

    tiles = []
    for k in range(cols_dev // B):
        j = k % n_src
        lt = k // n_src
        tiles.append(packet[:, j * window_cols + lt * B: j * window_cols + (lt + 1) * B])
    window_t = jnp.concatenate(tiles, axis=1)

    def apply(x):
        return lax.dot(inverse, x, precision=lax.Precision.HIGHEST,
                       preferred_element_type=jnp.float32)

    col_t = apply(window_t)
    col_t = jnp.concatenate(
        [jnp.where(col_id == 0, factor.T, col_t[:, :B]), col_t[:, B:]], axis=1
    )
    lower_t = apply(panel_t)
    lower_t = jnp.concatenate(
        [jnp.where(row_id == 0, factor.T, lower_t[:, :B]), lower_t[:, B:]], axis=1
    )
    change = lax.dot_general(
        lower_t,
        col_t,
        (((0,), (0,)), ((), ())),
        precision=lax.Precision.HIGHEST,
        preferred_element_type=jnp.float32,
    )
    local_rows = jnp.arange(rows_dev, dtype=jnp.int32)
    keep_rows = jnp.logical_and(row_id == 0, local_rows < B)
    stepped = jnp.where(keep_rows[:, None], matrix, matrix - change)
    first_cols = jnp.where(col_id == 0, lower_t.T, stepped[:, :B])
    return jnp.concatenate([first_cols, stepped[:, B:]], axis=1)


def solution(mesh):
    placed = (P("row", "col"),)
    return jax.shard_map(
        shards, mesh=mesh, in_specs=placed, out_specs=P("row", "col"), check_vma=False
    )
```

```python
import jax
import jax.numpy as jnp
from jax import lax
from jax.sharding import PartitionSpec as P

B = 64
RADIX = 2


def tree_broadcast(x, axes, size, index_of, member, radix=RADIX, have=1):
    while have < size:
        fresh = x
        for c in range(1, radix):
            lo = c * have
            if lo >= size:
                break
            pairs = []
            for src in index_of(None):
                for m in range(have):
                    if m + lo < size:
                        pairs.append((src(m), src(m + lo)))
            got = lax.ppermute(x, axes, pairs)
            take = jnp.logical_and(member >= lo, member < lo + have)
            fresh = jnp.where(take, got, fresh)
        x = fresh
        have *= radix
    return x


def shards(matrix):
    rows_dev, cols_dev = matrix.shape
    n_row = lax.axis_size("row")
    n_col = lax.axis_size("col")
    row_id = lax.axis_index("row")
    col_id = lax.axis_index("col")
    n_src = n_row // n_col
    window_cols = cols_dev * n_col // n_row

    panel_t = matrix[:, :B].T
    head = panel_t[:, :window_cols]

    def col0_group(_):
        return [lambda m: m * n_col]

    corner_t = tree_broadcast(panel_t[:, :B], ("row", "col"), n_row, col0_group, row_id, radix=4)

    def col_groups(_):
        return [lambda m, r=r: r * n_col + m for r in range(n_row)]

    panel_t, corner_t = lax.optimization_barrier((panel_t, corner_t))
    panel_t = tree_broadcast(panel_t, ("row", "col"), 2, col_groups, col_id, radix=2, have=1)

    rel = (row_id - col_id) % n_row
    my_j = rel // n_col
    is_src = rel % n_col == 0
    first = jnp.concatenate([head, corner_t], axis=1)
    pieces = []
    for c in range(n_src):
        pairs = []
        for r in range(n_row):
            q = r % n_col
            if c or q:
                pairs.append((r * n_col, ((r + n_col * c) % n_row) * n_col + q))
        got = lax.ppermute(first, ("row", "col"), pairs)
        if c == 0:
            got = jnp.where(col_id == 0, first, got)
        pieces.append(got)
    panel_t, pieces = lax.optimization_barrier((panel_t, pieces))
    panel_t = tree_broadcast(panel_t, ("row", "col"), n_col // 2, col_groups, col_id, radix=2, have=2)
    corner_t = pieces[0][:, window_cols:]
    pieces = [p[:, :window_cols] for p in pieces]
    ordered = []
    for jj in range(n_src):
        pick = pieces[0]
        for c in range(1, n_src):
            pick = jnp.where((my_j - jj) % n_src == c, pieces[c], pick)
        ordered.append(pick)
    packet = jnp.concatenate(ordered + [corner_t], axis=1)
    packet = jnp.where(is_src, packet, jnp.zeros_like(packet))

    def row_groups(_):
        out = []
        for q in range(n_col):
            for j in range(n_src):
                base = q + n_col * j
                out.append(lambda m, base=base, q=q: ((base + m) % n_row) * n_col + q)
        return out

    packet = tree_broadcast(packet, ("row", "col"), n_col, row_groups, rel % n_col)
    panel_t = tree_broadcast(panel_t, ("row", "col"), n_col, col_groups, col_id, radix=2, have=n_col // 2)
    panel_t, packet = lax.optimization_barrier((panel_t, packet))

    corner_t = packet[:, n_src * window_cols:]
    corner = (corner_t + corner_t.T) / 2.0
    factor = jnp.linalg.cholesky(corner)
    inverse = lax.linalg.triangular_solve(
        factor, jnp.eye(B, dtype=factor.dtype), left_side=True, lower=True
    )

    tiles = []
    for k in range(cols_dev // B):
        j = k % n_src
        lt = k // n_src
        tiles.append(packet[:, j * window_cols + lt * B: j * window_cols + (lt + 1) * B])
    window_t = jnp.concatenate(tiles, axis=1)

    def apply(x):
        return lax.dot(inverse, x, precision=lax.Precision.HIGHEST,
                       preferred_element_type=jnp.float32)

    col_t = apply(window_t)
    col_t = jnp.concatenate(
        [jnp.where(col_id == 0, factor.T, col_t[:, :B]), col_t[:, B:]], axis=1
    )
    lower_t = apply(panel_t)
    lower_t = jnp.concatenate(
        [jnp.where(row_id == 0, factor.T, lower_t[:, :B]), lower_t[:, B:]], axis=1
    )
    change = lax.dot_general(
        lower_t,
        col_t,
        (((0,), (0,)), ((), ())),
        precision=lax.Precision.HIGHEST,
        preferred_element_type=jnp.float32,
    )
    local_rows = jnp.arange(rows_dev, dtype=jnp.int32)
    keep_rows = jnp.logical_and(row_id == 0, local_rows < B)
    stepped = jnp.where(keep_rows[:, None], matrix, matrix - change)
    first_cols = jnp.where(col_id == 0, lower_t.T, stepped[:, :B])
    return jnp.concatenate([first_cols, stepped[:, B:]], axis=1)


def solution(mesh):
    placed = (P("row", "col"),)
    return jax.shard_map(
        shards, mesh=mesh, in_specs=placed, out_specs=P("row", "col"), check_vma=False
    )
```

```python
import jax
import jax.numpy as jnp
from jax import lax
from jax.sharding import PartitionSpec as P

B = 64
RADIX = 2


def tree_broadcast(x, axes, size, index_of, member, radix=RADIX, have=1):
    while have < size:
        fresh = x
        for c in range(1, radix):
            lo = c * have
            if lo >= size:
                break
            pairs = []
            for src in index_of(None):
                for m in range(have):
                    if m + lo < size:
                        pairs.append((src(m), src(m + lo)))
            got = lax.ppermute(x, axes, pairs)
            take = jnp.logical_and(member >= lo, member < lo + have)
            fresh = jnp.where(take, got, fresh)
        x = fresh
        have *= radix
    return x


def shards(matrix):
    rows_dev, cols_dev = matrix.shape
    n_row = lax.axis_size("row")
    n_col = lax.axis_size("col")
    row_id = lax.axis_index("row")
    col_id = lax.axis_index("col")
    n_src = n_row // n_col
    window_cols = cols_dev * n_col // n_row

    panel_t = matrix[:, :B].T
    head = panel_t[:, :window_cols]

    def col0_group(_):
        return [lambda m: m * n_col]

    corner_t = tree_broadcast(panel_t[:, :B], ("row", "col"), n_row, col0_group, row_id, radix=4)

    def col_groups(_):
        return [lambda m, r=r: r * n_col + m for r in range(n_row)]

    panel_t = tree_broadcast(panel_t, ("row", "col"), 2, col_groups, col_id, radix=2, have=1)

    rel = (row_id - col_id) % n_row
    my_j = rel // n_col
    is_src = rel % n_col == 0
    corner = (corner_t + corner_t.T) / 2.0
    factor = jnp.linalg.cholesky(corner)
    inverse = lax.linalg.triangular_solve(
        factor, jnp.eye(B, dtype=factor.dtype), left_side=True, lower=True
    )
    first = jnp.concatenate([head, factor.T, inverse], axis=1)
    pieces = []
    for c in range(n_src):
        pairs = []
        for r in range(n_row):
            q = r % n_col
            if c or q:
                pairs.append((r * n_col, ((r + n_col * c) % n_row) * n_col + q))
        got = lax.ppermute(first, ("row", "col"), pairs)
        if c == 0:
            got = jnp.where(col_id == 0, first, got)
        pieces.append(got)
    panel_t, pieces = lax.optimization_barrier((panel_t, pieces))
    panel_t = tree_broadcast(panel_t, ("row", "col"), n_col, col_groups, col_id, radix=2, have=2)
    fpack = pieces[0][:, window_cols:]
    pieces = [p[:, :window_cols] for p in pieces]
    ordered = []
    for jj in range(n_src):
        pick = pieces[0]
        for c in range(1, n_src):
            pick = jnp.where((my_j - jj) % n_src == c, pieces[c], pick)
        ordered.append(pick)
    packet = jnp.concatenate(ordered + [fpack], axis=1)
    packet = jnp.where(is_src, packet, jnp.zeros_like(packet))

    def row_groups(_):
        out = []
        for q in range(n_col):
            for j in range(n_src):
                base = q + n_col * j
                out.append(lambda m, base=base, q=q: ((base + m) % n_row) * n_col + q)
        return out

    packet = tree_broadcast(packet, ("row", "col"), n_col, row_groups, rel % n_col)
    factor_t = packet[:, n_src * window_cols: n_src * window_cols + B]
    inverse = packet[:, n_src * window_cols + B:]

    tiles = []
    for k in range(cols_dev // B):
        j = k % n_src
        lt = k // n_src
        tiles.append(packet[:, j * window_cols + lt * B: j * window_cols + (lt + 1) * B])
    window_t = jnp.concatenate(tiles, axis=1)

    def apply(x):
        return lax.dot(inverse, x, precision=lax.Precision.HIGHEST,
                       preferred_element_type=jnp.float32)

    col_t = apply(window_t)
    col_t = jnp.concatenate(
        [jnp.where(col_id == 0, factor_t, col_t[:, :B]), col_t[:, B:]], axis=1
    )
    lower_t = apply(panel_t)
    lower_t = jnp.concatenate(
        [jnp.where(row_id == 0, factor_t, lower_t[:, :B]), lower_t[:, B:]], axis=1
    )
    change = lax.dot_general(
        lower_t,
        col_t,
        (((0,), (0,)), ((), ())),
        precision=lax.Precision.HIGHEST,
        preferred_element_type=jnp.float32,
    )
    local_rows = jnp.arange(rows_dev, dtype=jnp.int32)
    keep_rows = jnp.logical_and(row_id == 0, local_rows < B)
    stepped = jnp.where(keep_rows[:, None], matrix, matrix - change)
    first_cols = jnp.where(col_id == 0, lower_t.T, stepped[:, :B])
    return jnp.concatenate([first_cols, stepped[:, B:]], axis=1)


def solution(mesh):
    placed = (P("row", "col"),)
    return jax.shard_map(
        shards, mesh=mesh, in_specs=placed, out_specs=P("row", "col"), check_vma=False
    )
```

```python
import jax
import jax.numpy as jnp
from jax import lax
from jax.sharding import PartitionSpec as P

B = 64
RADIX = 2


def tree_broadcast(x, axes, size, index_of, member, radix=RADIX, have=1):
    while have < size:
        fresh = x
        for c in range(1, radix):
            lo = c * have
            if lo >= size:
                break
            pairs = []
            for src in index_of(None):
                for m in range(have):
                    if m + lo < size:
                        pairs.append((src(m), src(m + lo)))
            got = lax.ppermute(x, axes, pairs)
            take = jnp.logical_and(member >= lo, member < lo + have)
            fresh = jnp.where(take, got, fresh)
        x = fresh
        have *= radix
    return x


def shards(matrix):
    rows_dev, cols_dev = matrix.shape
    n_row = lax.axis_size("row")
    n_col = lax.axis_size("col")
    row_id = lax.axis_index("row")
    col_id = lax.axis_index("col")
    n_src = n_row // n_col
    window_cols = cols_dev * n_col // n_row

    panel_t = matrix[:, :B].T
    head = panel_t[:, :window_cols]

    def col0_group(_):
        return [lambda m: m * n_col]

    corner_t = tree_broadcast(panel_t[:, :B], ("row", "col"), n_row, col0_group, row_id, radix=4)

    def col_groups(_):
        return [lambda m, r=r: r * n_col + m for r in range(n_row)]

    panel_t = tree_broadcast(panel_t, ("row", "col"), 2, col_groups, col_id, radix=2, have=1)

    rel = (row_id - col_id) % n_row
    my_j = rel // n_col
    is_src = rel % n_col == 0
    corner = (corner_t + corner_t.T) / 2.0
    factor = jnp.linalg.cholesky(corner)
    inverse = lax.linalg.triangular_solve(
        factor, jnp.eye(B, dtype=factor.dtype), left_side=True, lower=True
    )
    first = jnp.concatenate([head, factor.T, inverse], axis=1)
    pieces = []
    for c in range(n_src):
        pairs = []
        for r in range(n_row):
            q = r % n_col
            if c or q:
                pairs.append((r * n_col, ((r + n_col * c) % n_row) * n_col + q))
        got = lax.ppermute(first, ("row", "col"), pairs)
        if c == 0:
            got = jnp.where(col_id == 0, first, got)
        pieces.append(got)
    panel_t, pieces = lax.optimization_barrier((panel_t, pieces))
    panel_t = tree_broadcast(panel_t, ("row", "col"), n_col // 2, col_groups, col_id, radix=2, have=2)
    fpack = pieces[0][:, window_cols:]
    pieces = [p[:, :window_cols] for p in pieces]
    ordered = []
    for jj in range(n_src):
        pick = pieces[0]
        for c in range(1, n_src):
            pick = jnp.where((my_j - jj) % n_src == c, pieces[c], pick)
        ordered.append(pick)
    packet = jnp.concatenate(ordered + [fpack], axis=1)
    packet = jnp.where(is_src, packet, jnp.zeros_like(packet))

    def row_groups(_):
        out = []
        for q in range(n_col):
            for j in range(n_src):
                base = q + n_col * j
                out.append(lambda m, base=base, q=q: ((base + m) % n_row) * n_col + q)
        return out

    packet = tree_broadcast(packet, ("row", "col"), n_col, row_groups, rel % n_col)
    panel_t = tree_broadcast(panel_t, ("row", "col"), n_col, col_groups, col_id, radix=2, have=n_col // 2)
    panel_t, packet = lax.optimization_barrier((panel_t, packet))
    factor_t = packet[:, n_src * window_cols: n_src * window_cols + B]
    inverse = packet[:, n_src * window_cols + B:]

    tiles = []
    for k in range(cols_dev // B):
        j = k % n_src
        lt = k // n_src
        tiles.append(packet[:, j * window_cols + lt * B: j * window_cols + (lt + 1) * B])
    window_t = jnp.concatenate(tiles, axis=1)

    def apply(x):
        return lax.dot(inverse, x, precision=lax.Precision.HIGHEST,
                       preferred_element_type=jnp.float32)

    col_t = apply(window_t)
    col_t = jnp.concatenate(
        [jnp.where(col_id == 0, factor_t, col_t[:, :B]), col_t[:, B:]], axis=1
    )
    lower_t = apply(panel_t)
    lower_t = jnp.concatenate(
        [jnp.where(row_id == 0, factor_t, lower_t[:, :B]), lower_t[:, B:]], axis=1
    )
    change = lax.dot_general(
        lower_t,
        col_t,
        (((0,), (0,)), ((), ())),
        precision=lax.Precision.HIGHEST,
        preferred_element_type=jnp.float32,
    )
    local_rows = jnp.arange(rows_dev, dtype=jnp.int32)
    keep_rows = jnp.logical_and(row_id == 0, local_rows < B)
    stepped = jnp.where(keep_rows[:, None], matrix, matrix - change)
    first_cols = jnp.where(col_id == 0, lower_t.T, stepped[:, :B])
    return jnp.concatenate([first_cols, stepped[:, B:]], axis=1)


def solution(mesh):
    placed = (P("row", "col"),)
    return jax.shard_map(
        shards, mesh=mesh, in_specs=placed, out_specs=P("row", "col"), check_vma=False
    )
```

```python
import jax
import jax.numpy as jnp
from jax import lax
from jax.sharding import PartitionSpec as P

B = 64
RADIX = 2


def tree_broadcast(x, axes, size, index_of, member, radix=RADIX, have=1):
    while have < size:
        fresh = x
        for c in range(1, radix):
            lo = c * have
            if lo >= size:
                break
            pairs = []
            for src in index_of(None):
                for m in range(have):
                    if m + lo < size:
                        pairs.append((src(m), src(m + lo)))
            got = lax.ppermute(x, axes, pairs)
            take = jnp.logical_and(member >= lo, member < lo + have)
            fresh = jnp.where(take, got, fresh)
        x = fresh
        have *= radix
    return x


def shards(matrix):
    rows_dev, cols_dev = matrix.shape
    n_row = lax.axis_size("row")
    n_col = lax.axis_size("col")
    row_id = lax.axis_index("row")
    col_id = lax.axis_index("col")
    n_src = n_row // n_col
    window_cols = cols_dev * n_col // n_row

    panel_t = matrix[:, :B].T
    head = panel_t[:, :window_cols]

    def col_groups(_):
        return [lambda m, r=r: r * n_col + m for r in range(n_row)]

    panel_t = tree_broadcast(panel_t, ("row", "col"), 2, col_groups, col_id, radix=2, have=1)

    rel = (row_id - col_id) % n_row
    my_j = rel // n_col
    is_src = rel % n_col == 0
    pieces = []
    for c in range(n_src):
        pairs = []
        for r in range(n_row):
            q = r % n_col
            if c or q:
                pairs.append((r * n_col, ((r + n_col * c) % n_row) * n_col + q))
        got = lax.ppermute(head, ("row", "col"), pairs)
        if c == 0:
            got = jnp.where(col_id == 0, head, got)
        pieces.append(got)

    corner_t = panel_t[:, :B]
    corner = (corner_t + corner_t.T) / 2.0
    factor = jnp.linalg.cholesky(corner)
    inverse = lax.linalg.triangular_solve(
        factor, jnp.eye(B, dtype=factor.dtype), left_side=True, lower=True
    )
    fpack = jnp.concatenate([factor.T, inverse], axis=1)

    def src_group(_):
        return [lambda m: m * n_col + m % n_col]

    src_member = jnp.where(is_src, row_id, n_row)
    fpack = tree_broadcast(fpack, ("row", "col"), n_row, src_group, src_member, radix=4)

    panel_t, pieces = lax.optimization_barrier((panel_t, pieces))
    panel_t = tree_broadcast(panel_t, ("row", "col"), n_col // 2, col_groups, col_id, radix=2, have=2)
    ordered = []
    for jj in range(n_src):
        pick = pieces[0]
        for c in range(1, n_src):
            pick = jnp.where((my_j - jj) % n_src == c, pieces[c], pick)
        ordered.append(pick)
    packet = jnp.concatenate(ordered + [fpack], axis=1)
    packet = jnp.where(is_src, packet, jnp.zeros_like(packet))

    def row_groups(_):
        out = []
        for q in range(n_col):
            for j in range(n_src):
                base = q + n_col * j
                out.append(lambda m, base=base, q=q: ((base + m) % n_row) * n_col + q)
        return out

    packet = tree_broadcast(packet, ("row", "col"), n_col, row_groups, rel % n_col)
    panel_t = tree_broadcast(panel_t, ("row", "col"), n_col, col_groups, col_id, radix=2, have=n_col // 2)
    panel_t, packet = lax.optimization_barrier((panel_t, packet))
    factor_t = packet[:, n_src * window_cols: n_src * window_cols + B]
    inverse = packet[:, n_src * window_cols + B:]

    tiles = []
    for k in range(cols_dev // B):
        j = k % n_src
        lt = k // n_src
        tiles.append(packet[:, j * window_cols + lt * B: j * window_cols + (lt + 1) * B])
    window_t = jnp.concatenate(tiles, axis=1)

    def apply(x):
        return lax.dot(inverse, x, precision=lax.Precision.HIGHEST,
                       preferred_element_type=jnp.float32)

    col_t = apply(window_t)
    col_t = jnp.concatenate(
        [jnp.where(col_id == 0, factor_t, col_t[:, :B]), col_t[:, B:]], axis=1
    )
    lower_t = apply(panel_t)
    lower_t = jnp.concatenate(
        [jnp.where(row_id == 0, factor_t, lower_t[:, :B]), lower_t[:, B:]], axis=1
    )
    change = lax.dot_general(
        lower_t,
        col_t,
        (((0,), (0,)), ((), ())),
        precision=lax.Precision.HIGHEST,
        preferred_element_type=jnp.float32,
    )
    local_rows = jnp.arange(rows_dev, dtype=jnp.int32)
    keep_rows = jnp.logical_and(row_id == 0, local_rows < B)
    stepped = jnp.where(keep_rows[:, None], matrix, matrix - change)
    first_cols = jnp.where(col_id == 0, lower_t.T, stepped[:, :B])
    return jnp.concatenate([first_cols, stepped[:, B:]], axis=1)


def solution(mesh):
    placed = (P("row", "col"),)
    return jax.shard_map(
        shards, mesh=mesh, in_specs=placed, out_specs=P("row", "col"), check_vma=False
    )
```

```python
import jax
import jax.numpy as jnp
from jax import lax
from jax.sharding import PartitionSpec as P

B = 64
RADIX = 2


def tree_broadcast(x, axes, size, index_of, member, radix=RADIX, have=1):
    while have < size:
        fresh = x
        for c in range(1, radix):
            lo = c * have
            if lo >= size:
                break
            pairs = []
            for src in index_of(None):
                for m in range(have):
                    if m + lo < size:
                        pairs.append((src(m), src(m + lo)))
            got = lax.ppermute(x, axes, pairs)
            take = jnp.logical_and(member >= lo, member < lo + have)
            fresh = jnp.where(take, got, fresh)
        x = fresh
        have *= radix
    return x


def shards(matrix):
    rows_dev, cols_dev = matrix.shape
    n_row = lax.axis_size("row")
    n_col = lax.axis_size("col")
    row_id = lax.axis_index("row")
    col_id = lax.axis_index("col")
    n_src = n_row // n_col
    window_cols = cols_dev * n_col // n_row

    panel_t = matrix[:, :B].T
    head = panel_t[:, :window_cols]

    def col0_group(_):
        return [lambda m: m * n_col]

    corner_t = tree_broadcast(panel_t[:, :B], ("row", "col"), n_row, col0_group, row_id, radix=4)

    def col_groups(_):
        return [lambda m, r=r: r * n_col + m for r in range(n_row)]

    panel_t = tree_broadcast(panel_t, ("row", "col"), 2, col_groups, col_id, radix=2, have=1)

    rel = (row_id - col_id) % n_row
    my_j = rel // n_col
    is_src = rel % n_col == 0
    corner = (corner_t + corner_t.T) / 2.0
    factor = jnp.linalg.cholesky(corner)
    inverse = lax.linalg.triangular_solve(
        factor, jnp.eye(B, dtype=factor.dtype), left_side=True, lower=True
    )
    first = jnp.concatenate([head, factor.T, inverse], axis=1)
    pieces = []
    for c in range(n_src):
        pairs = []
        for r in range(n_row):
            q = r % n_col
            if c or q:
                pairs.append((r * n_col, ((r + n_col * c) % n_row) * n_col + q))
        got = lax.ppermute(first, ("row", "col"), pairs)
        if c == 0:
            got = jnp.where(col_id == 0, first, got)
        pieces.append(got)
    panel_t, pieces = lax.optimization_barrier((panel_t, pieces))
    panel_t = tree_broadcast(panel_t, ("row", "col"), n_col // 2, col_groups, col_id, radix=2, have=2)
    fpack = pieces[0][:, window_cols:]
    pieces = [p[:, :window_cols] for p in pieces]
    ordered = []
    for jj in range(n_src):
        pick = pieces[0]
        for c in range(1, n_src):
            pick = jnp.where((my_j - jj) % n_src == c, pieces[c], pick)
        ordered.append(pick)
    packet = jnp.concatenate(ordered + [fpack], axis=1)
    packet = jnp.where(is_src, packet, jnp.zeros_like(packet))

    def row_groups(_):
        out = []
        for q in range(n_col):
            for j in range(n_src):
                base = q + n_col * j
                out.append(lambda m, base=base, q=q: ((base + m) % n_row) * n_col + q)
        return out

    packet = tree_broadcast(packet, ("row", "col"), n_col, row_groups, rel % n_col)
    panel_t = tree_broadcast(panel_t, ("row", "col"), n_col, col_groups, col_id, radix=2, have=n_col // 2)
    panel_t, packet = lax.optimization_barrier((panel_t, packet))
    factor_t = packet[:, n_src * window_cols: n_src * window_cols + B]
    inverse = packet[:, n_src * window_cols + B:]

    tiles = []
    for k in range(cols_dev // B):
        j = k % n_src
        lt = k // n_src
        tiles.append(packet[:, j * window_cols + lt * B: j * window_cols + (lt + 1) * B])
    window_t = jnp.concatenate(tiles, axis=1)

    def apply(x):
        return lax.dot(inverse, x, precision=lax.Precision.HIGHEST,
                       preferred_element_type=jnp.float32)

    col_t = apply(window_t)
    col_t = lax.dynamic_update_slice(
        col_t, jnp.where(col_id == 0, factor_t, col_t[:, :B]), (0, 0)
    )
    lower_t = apply(panel_t)
    lower_t = lax.dynamic_update_slice(
        lower_t, jnp.where(row_id == 0, factor_t, lower_t[:, :B]), (0, 0)
    )
    change = lax.dot_general(
        lower_t,
        col_t,
        (((0,), (0,)), ((), ())),
        precision=lax.Precision.HIGHEST,
        preferred_element_type=jnp.float32,
    )
    local_rows = jnp.arange(rows_dev, dtype=jnp.int32)
    keep_rows = jnp.logical_and(row_id == 0, local_rows < B)
    stepped = jnp.where(keep_rows[:, None], matrix, matrix - change)
    first_cols = jnp.where(col_id == 0, lower_t.T, stepped[:, :B])
    return lax.dynamic_update_slice(stepped, first_cols, (0, 0))


def solution(mesh):
    placed = (P("row", "col"),)
    return jax.shard_map(
        shards, mesh=mesh, in_specs=placed, out_specs=P("row", "col"), check_vma=False
    )
```

```python
import jax
import jax.numpy as jnp
from jax import lax
from jax.sharding import PartitionSpec as P

B = 64
RADIX = 2


def tree_broadcast(x, axes, size, index_of, member, radix=RADIX, have=1):
    while have < size:
        fresh = x
        for c in range(1, radix):
            lo = c * have
            if lo >= size:
                break
            pairs = []
            for src in index_of(None):
                for m in range(have):
                    if m + lo < size:
                        pairs.append((src(m), src(m + lo)))
            got = lax.ppermute(x, axes, pairs)
            take = jnp.logical_and(member >= lo, member < lo + have)
            fresh = jnp.where(take, got, fresh)
        x = fresh
        have *= radix
    return x


def shards(matrix):
    rows_dev, cols_dev = matrix.shape
    n_row = lax.axis_size("row")
    n_col = lax.axis_size("col")
    row_id = lax.axis_index("row")
    col_id = lax.axis_index("col")
    n_src = n_row // n_col
    window_cols = cols_dev * n_col // n_row

    panel_t = matrix[:, :B].T
    head = panel_t[:, :window_cols]

    def col0_group(_):
        return [lambda m: m * n_col]

    corner_t = tree_broadcast(panel_t[:, :B], ("row", "col"), n_row, col0_group, row_id, radix=4)

    bits = n_col.bit_length() - 1

    def spread(m):
        out = m & 1
        for b in range(1, bits):
            out = out | (((m >> b) & 1) << (bits - b))
        return out

    def col_groups(_):
        return [lambda m, r=r: r * n_col + spread(m) for r in range(n_row)]

    col_member = spread(col_id)

    panel_t = tree_broadcast(panel_t, ("row", "col"), 2, col_groups, col_member, radix=2, have=1)

    rel = (row_id - col_id) % n_row
    my_j = rel // n_col
    is_src = rel % n_col == 0
    corner = (corner_t + corner_t.T) / 2.0
    factor = jnp.linalg.cholesky(corner)
    inverse = lax.linalg.triangular_solve(
        factor, jnp.eye(B, dtype=factor.dtype), left_side=True, lower=True
    )
    first = jnp.concatenate([head, factor.T, inverse], axis=1)
    pieces = []
    for c in range(n_src):
        pairs = []
        for r in range(n_row):
            q = r % n_col
            if c or q:
                pairs.append((r * n_col, ((r + n_col * c) % n_row) * n_col + q))
        got = lax.ppermute(first, ("row", "col"), pairs)
        if c == 0:
            got = jnp.where(col_id == 0, first, got)
        pieces.append(got)
    panel_t, pieces = lax.optimization_barrier((panel_t, pieces))
    panel_t = tree_broadcast(panel_t, ("row", "col"), n_col // 2, col_groups, col_member, radix=2, have=2)
    fpack = pieces[0][:, window_cols:]
    pieces = [p[:, :window_cols] for p in pieces]
    ordered = []
    for jj in range(n_src):
        pick = pieces[0]
        for c in range(1, n_src):
            pick = jnp.where((my_j - jj) % n_src == c, pieces[c], pick)
        ordered.append(pick)
    packet = jnp.concatenate(ordered + [fpack], axis=1)
    packet = jnp.where(is_src, packet, jnp.zeros_like(packet))

    def row_groups(_):
        out = []
        for q in range(n_col):
            for j in range(n_src):
                base = q + n_col * j
                out.append(lambda m, base=base, q=q: ((base + m) % n_row) * n_col + q)
        return out

    packet = tree_broadcast(packet, ("row", "col"), n_col, row_groups, rel % n_col)
    panel_t = tree_broadcast(panel_t, ("row", "col"), n_col, col_groups, col_member, radix=2, have=n_col // 2)
    panel_t, packet = lax.optimization_barrier((panel_t, packet))
    factor_t = packet[:, n_src * window_cols: n_src * window_cols + B]
    inverse = packet[:, n_src * window_cols + B:]

    tiles = []
    for k in range(cols_dev // B):
        j = k % n_src
        lt = k // n_src
        tiles.append(packet[:, j * window_cols + lt * B: j * window_cols + (lt + 1) * B])
    window_t = jnp.concatenate(tiles, axis=1)

    def apply(x):
        return lax.dot(inverse, x, precision=lax.Precision.HIGHEST,
                       preferred_element_type=jnp.float32)

    col_t = apply(window_t)
    col_t = jnp.concatenate(
        [jnp.where(col_id == 0, factor_t, col_t[:, :B]), col_t[:, B:]], axis=1
    )
    lower_t = apply(panel_t)
    lower_t = jnp.concatenate(
        [jnp.where(row_id == 0, factor_t, lower_t[:, :B]), lower_t[:, B:]], axis=1
    )
    change = lax.dot_general(
        lower_t,
        col_t,
        (((0,), (0,)), ((), ())),
        precision=lax.Precision.HIGHEST,
        preferred_element_type=jnp.float32,
    )
    local_rows = jnp.arange(rows_dev, dtype=jnp.int32)
    keep_rows = jnp.logical_and(row_id == 0, local_rows < B)
    stepped = jnp.where(keep_rows[:, None], matrix, matrix - change)
    first_cols = jnp.where(col_id == 0, lower_t.T, stepped[:, :B])
    return jnp.concatenate([first_cols, stepped[:, B:]], axis=1)


def solution(mesh):
    placed = (P("row", "col"),)
    return jax.shard_map(
        shards, mesh=mesh, in_specs=placed, out_specs=P("row", "col"), check_vma=False
    )
```

```python
import jax
import jax.numpy as jnp
from jax import lax
from jax.sharding import PartitionSpec as P

B = 64
RADIX = 2


def tree_broadcast(x, axes, size, index_of, member, radix=RADIX, have=1):
    while have < size:
        fresh = x
        for c in range(1, radix):
            lo = c * have
            if lo >= size:
                break
            pairs = []
            for src in index_of(None):
                for m in range(have):
                    if m + lo < size:
                        pairs.append((src(m), src(m + lo)))
            got = lax.ppermute(x, axes, pairs)
            take = jnp.logical_and(member >= lo, member < lo + have)
            fresh = jnp.where(take, got, fresh)
        x = fresh
        have *= radix
    return x


def shards(matrix):
    rows_dev, cols_dev = matrix.shape
    n_row = lax.axis_size("row")
    n_col = lax.axis_size("col")
    row_id = lax.axis_index("row")
    col_id = lax.axis_index("col")
    n_src = n_row // n_col
    window_cols = cols_dev * n_col // n_row

    panel_t = matrix[:, :B].T
    head = panel_t[:, :window_cols]

    def col0_group(_):
        return [lambda m: m * n_col]

    corner_t = tree_broadcast(panel_t[:, :B], ("row", "col"), n_row, col0_group, row_id, radix=4)

    bits = n_col.bit_length() - 1

    def spread(m):
        out = m & 1
        for b in range(1, bits):
            out = out | (((m >> b) & 1) << (bits - b))
        return out

    def col_groups(_):
        return [lambda m, r=r: r * n_col + spread(m) for r in range(n_row)]

    col_member = spread(col_id)

    panel_t = tree_broadcast(panel_t, ("row", "col"), 2, col_groups, col_member, radix=2, have=1)

    rel = (row_id - col_id) % n_row
    my_j = rel // n_col
    is_src = rel % n_col == 0
    corner = (corner_t + corner_t.T) / 2.0
    factor = jnp.linalg.cholesky(corner)
    inverse = lax.linalg.triangular_solve(
        factor, jnp.eye(B, dtype=factor.dtype), left_side=True, lower=True
    )
    first = jnp.concatenate([head, factor.T, inverse], axis=1)
    pieces = []
    for c in range(n_src):
        pairs = []
        for r in range(n_row):
            q = r % n_col
            if c or q:
                pairs.append((r * n_col, ((r + n_col * c) % n_row) * n_col + q))
        got = lax.ppermute(first, ("row", "col"), pairs)
        if c == 0:
            got = jnp.where(col_id == 0, first, got)
        pieces.append(got)
    panel_t, pieces = lax.optimization_barrier((panel_t, pieces))
    panel_t = tree_broadcast(panel_t, ("row", "col"), n_col // 2, col_groups, col_member, radix=2, have=2)
    fpack = pieces[0][:, window_cols:]
    pieces = [p[:, :window_cols] for p in pieces]
    ordered = []
    for jj in range(n_src):
        pick = pieces[0]
        for c in range(1, n_src):
            pick = jnp.where((my_j - jj) % n_src == c, pieces[c], pick)
        ordered.append(pick)
    packet = jnp.concatenate(ordered + [fpack], axis=1)
    packet = jnp.where(is_src, packet, jnp.zeros_like(packet))

    def flip(m):
        out = 0
        for b in range(bits):
            out = out | (((m >> b) & 1) << (bits - 1 - b))
        return out

    def row_groups(_):
        out = []
        for q in range(n_col):
            for j in range(n_src):
                base = q + n_col * j
                out.append(lambda m, base=base, q=q: ((base + flip(m)) % n_row) * n_col + q)
        return out

    packet = tree_broadcast(packet, ("row", "col"), n_col, row_groups, flip(rel % n_col))
    panel_t = tree_broadcast(panel_t, ("row", "col"), n_col, col_groups, col_member, radix=2, have=n_col // 2)
    panel_t, packet = lax.optimization_barrier((panel_t, packet))
    factor_t = packet[:, n_src * window_cols: n_src * window_cols + B]
    inverse = packet[:, n_src * window_cols + B:]

    tiles = []
    for k in range(cols_dev // B):
        j = k % n_src
        lt = k // n_src
        tiles.append(packet[:, j * window_cols + lt * B: j * window_cols + (lt + 1) * B])
    window_t = jnp.concatenate(tiles, axis=1)

    def apply(x):
        return lax.dot(inverse, x, precision=lax.Precision.HIGHEST,
                       preferred_element_type=jnp.float32)

    col_t = apply(window_t)
    col_t = jnp.concatenate(
        [jnp.where(col_id == 0, factor_t, col_t[:, :B]), col_t[:, B:]], axis=1
    )
    lower_t = apply(panel_t)
    lower_t = jnp.concatenate(
        [jnp.where(row_id == 0, factor_t, lower_t[:, :B]), lower_t[:, B:]], axis=1
    )
    change = lax.dot_general(
        lower_t,
        col_t,
        (((0,), (0,)), ((), ())),
        precision=lax.Precision.HIGHEST,
        preferred_element_type=jnp.float32,
    )
    local_rows = jnp.arange(rows_dev, dtype=jnp.int32)
    keep_rows = jnp.logical_and(row_id == 0, local_rows < B)
    stepped = jnp.where(keep_rows[:, None], matrix, matrix - change)
    first_cols = jnp.where(col_id == 0, lower_t.T, stepped[:, :B])
    return jnp.concatenate([first_cols, stepped[:, B:]], axis=1)


def solution(mesh):
    placed = (P("row", "col"),)
    return jax.shard_map(
        shards, mesh=mesh, in_specs=placed, out_specs=P("row", "col"), check_vma=False
    )
```

```python
import jax
import jax.numpy as jnp
from jax import lax
from jax.sharding import PartitionSpec as P

B = 64
RADIX = 2


def tree_broadcast(x, axes, size, index_of, member, radix=RADIX, have=1):
    while have < size:
        fresh = x
        for c in range(1, radix):
            lo = c * have
            if lo >= size:
                break
            pairs = []
            for src in index_of(None):
                for m in range(have):
                    if m + lo < size:
                        pairs.append((src(m), src(m + lo)))
            got = lax.ppermute(x, axes, pairs)
            take = jnp.logical_and(member >= lo, member < lo + have)
            fresh = jnp.where(take, got, fresh)
        x = fresh
        have *= radix
    return x


def shards(matrix):
    rows_dev, cols_dev = matrix.shape
    n_row = lax.axis_size("row")
    n_col = lax.axis_size("col")
    row_id = lax.axis_index("row")
    col_id = lax.axis_index("col")
    n_src = n_row // n_col
    window_cols = cols_dev * n_col // n_row

    panel_t = matrix[:, :B].T
    head = panel_t[:, :window_cols]

    def col0_group(_):
        return [lambda m: m * n_col]

    corner_t = tree_broadcast(panel_t[:, :B], ("row", "col"), n_row, col0_group, row_id, radix=4)

    bits = n_col.bit_length() - 1

    def spread(m):
        out = m & 1
        for b in range(1, bits):
            out = out | (((m >> b) & 1) << (bits - b))
        return out

    def col_groups(_):
        return [lambda m, r=r: r * n_col + spread(m) for r in range(n_row)]

    col_member = spread(col_id)

    panel_t = tree_broadcast(panel_t, ("row", "col"), 2, col_groups, col_member, radix=2, have=1)

    rel = (row_id - col_id) % n_row
    my_j = rel // n_col
    is_src = rel % n_col == 0
    corner = (corner_t + corner_t.T) / 2.0
    factor = jnp.linalg.cholesky(corner)
    inverse = lax.linalg.triangular_solve(
        factor, jnp.eye(B, dtype=factor.dtype), left_side=True, lower=True
    )
    first = jnp.concatenate([head, factor.T, inverse], axis=1)
    pieces = []
    for c in range(n_src):
        pairs = []
        for r in range(n_row):
            q = r % n_col
            if c or q:
                pairs.append((r * n_col, ((r + n_col * c) % n_row) * n_col + q))
        got = lax.ppermute(first, ("row", "col"), pairs)
        if c == 0:
            got = jnp.where(col_id == 0, first, got)
        pieces.append(got)
    panel_t, pieces = lax.optimization_barrier((panel_t, pieces))
    panel_t = tree_broadcast(panel_t, ("row", "col"), n_col // 2, col_groups, col_member, radix=2, have=2)
    fpack = pieces[0][:, window_cols:]
    pieces = [p[:, :window_cols] for p in pieces]
    ordered = []
    for jj in range(n_src):
        pick = pieces[0]
        for c in range(1, n_src):
            pick = jnp.where((my_j - jj) % n_src == c, pieces[c], pick)
        ordered.append(pick)
    packet = jnp.concatenate(ordered + [fpack], axis=1)
    packet = jnp.where(is_src, packet, jnp.zeros_like(packet))

    def row_groups(_):
        out = []
        for q in range(n_col):
            for j in range(n_src):
                base = q + n_col * j
                out.append(lambda m, base=base, q=q: ((base + m) % n_row) * n_col + q)
        return out

    packet = tree_broadcast(packet, ("row", "col"), n_col, row_groups, rel % n_col, radix=4)
    panel_t = tree_broadcast(panel_t, ("row", "col"), n_col, col_groups, col_member, radix=2, have=n_col // 2)
    panel_t, packet = lax.optimization_barrier((panel_t, packet))
    factor_t = packet[:, n_src * window_cols: n_src * window_cols + B]
    inverse = packet[:, n_src * window_cols + B:]

    tiles = []
    for k in range(cols_dev // B):
        j = k % n_src
        lt = k // n_src
        tiles.append(packet[:, j * window_cols + lt * B: j * window_cols + (lt + 1) * B])
    window_t = jnp.concatenate(tiles, axis=1)

    def apply(x):
        return lax.dot(inverse, x, precision=lax.Precision.HIGHEST,
                       preferred_element_type=jnp.float32)

    col_t = apply(window_t)
    col_t = jnp.concatenate(
        [jnp.where(col_id == 0, factor_t, col_t[:, :B]), col_t[:, B:]], axis=1
    )
    lower_t = apply(panel_t)
    lower_t = jnp.concatenate(
        [jnp.where(row_id == 0, factor_t, lower_t[:, :B]), lower_t[:, B:]], axis=1
    )
    change = lax.dot_general(
        lower_t,
        col_t,
        (((0,), (0,)), ((), ())),
        precision=lax.Precision.HIGHEST,
        preferred_element_type=jnp.float32,
    )
    local_rows = jnp.arange(rows_dev, dtype=jnp.int32)
    keep_rows = jnp.logical_and(row_id == 0, local_rows < B)
    stepped = jnp.where(keep_rows[:, None], matrix, matrix - change)
    first_cols = jnp.where(col_id == 0, lower_t.T, stepped[:, :B])
    return jnp.concatenate([first_cols, stepped[:, B:]], axis=1)


def solution(mesh):
    placed = (P("row", "col"),)
    return jax.shard_map(
        shards, mesh=mesh, in_specs=placed, out_specs=P("row", "col"), check_vma=False
    )
```

```python
import jax
import jax.numpy as jnp
from jax import lax
from jax.sharding import PartitionSpec as P

B = 64
RADIX = 2


def tree_broadcast(x, axes, size, index_of, member, radix=RADIX, have=1):
    while have < size:
        fresh = x
        for c in range(1, radix):
            lo = c * have
            if lo >= size:
                break
            pairs = []
            for src in index_of(None):
                for m in range(have):
                    if m + lo < size:
                        pairs.append((src(m), src(m + lo)))
            got = lax.ppermute(x, axes, pairs)
            take = jnp.logical_and(member >= lo, member < lo + have)
            fresh = jnp.where(take, got, fresh)
        x = fresh
        have *= radix
    return x


def shards(matrix):
    rows_dev, cols_dev = matrix.shape
    n_row = lax.axis_size("row")
    n_col = lax.axis_size("col")
    row_id = lax.axis_index("row")
    col_id = lax.axis_index("col")
    n_src = n_row // n_col
    window_cols = cols_dev * n_col // n_row

    panel_t = matrix[:, :B].T
    head = panel_t[:, :window_cols]

    def col0_group(_):
        return [lambda m: m * n_col]

    corner_t = tree_broadcast(panel_t[:, :B], ("row", "col"), n_row, col0_group, row_id, radix=8)

    bits = n_col.bit_length() - 1

    def spread(m):
        out = m & 1
        for b in range(1, bits):
            out = out | (((m >> b) & 1) << (bits - b))
        return out

    def col_groups(_):
        return [lambda m, r=r: r * n_col + spread(m) for r in range(n_row)]

    col_member = spread(col_id)

    panel_t = tree_broadcast(panel_t, ("row", "col"), 2, col_groups, col_member, radix=2, have=1)

    rel = (row_id - col_id) % n_row
    my_j = rel // n_col
    is_src = rel % n_col == 0
    corner = (corner_t + corner_t.T) / 2.0
    factor = jnp.linalg.cholesky(corner)
    inverse = lax.linalg.triangular_solve(
        factor, jnp.eye(B, dtype=factor.dtype), left_side=True, lower=True
    )
    first = jnp.concatenate([head, factor.T, inverse], axis=1)
    pieces = []
    for c in range(n_src):
        pairs = []
        for r in range(n_row):
            q = r % n_col
            if c or q:
                pairs.append((r * n_col, ((r + n_col * c) % n_row) * n_col + q))
        got = lax.ppermute(first, ("row", "col"), pairs)
        if c == 0:
            got = jnp.where(col_id == 0, first, got)
        pieces.append(got)
    panel_t, pieces = lax.optimization_barrier((panel_t, pieces))
    panel_t = tree_broadcast(panel_t, ("row", "col"), n_col // 2, col_groups, col_member, radix=2, have=2)
    fpack = pieces[0][:, window_cols:]
    pieces = [p[:, :window_cols] for p in pieces]
    ordered = []
    for jj in range(n_src):
        pick = pieces[0]
        for c in range(1, n_src):
            pick = jnp.where((my_j - jj) % n_src == c, pieces[c], pick)
        ordered.append(pick)
    packet = jnp.concatenate(ordered + [fpack], axis=1)
    packet = jnp.where(is_src, packet, jnp.zeros_like(packet))

    def row_groups(_):
        out = []
        for q in range(n_col):
            for j in range(n_src):
                base = q + n_col * j
                out.append(lambda m, base=base, q=q: ((base + m) % n_row) * n_col + q)
        return out

    packet = tree_broadcast(packet, ("row", "col"), n_col, row_groups, rel % n_col, radix=4)
    panel_t = tree_broadcast(panel_t, ("row", "col"), n_col, col_groups, col_member, radix=2, have=n_col // 2)
    panel_t, packet = lax.optimization_barrier((panel_t, packet))
    factor_t = packet[:, n_src * window_cols: n_src * window_cols + B]
    inverse = packet[:, n_src * window_cols + B:]

    tiles = []
    for k in range(cols_dev // B):
        j = k % n_src
        lt = k // n_src
        tiles.append(packet[:, j * window_cols + lt * B: j * window_cols + (lt + 1) * B])
    window_t = jnp.concatenate(tiles, axis=1)

    def apply(x):
        return lax.dot(inverse, x, precision=lax.Precision.HIGHEST,
                       preferred_element_type=jnp.float32)

    col_t = apply(window_t)
    col_t = jnp.concatenate(
        [jnp.where(col_id == 0, factor_t, col_t[:, :B]), col_t[:, B:]], axis=1
    )
    lower_t = apply(panel_t)
    lower_t = jnp.concatenate(
        [jnp.where(row_id == 0, factor_t, lower_t[:, :B]), lower_t[:, B:]], axis=1
    )
    change = lax.dot_general(
        lower_t,
        col_t,
        (((0,), (0,)), ((), ())),
        precision=lax.Precision.HIGHEST,
        preferred_element_type=jnp.float32,
    )
    local_rows = jnp.arange(rows_dev, dtype=jnp.int32)
    keep_rows = jnp.logical_and(row_id == 0, local_rows < B)
    stepped = jnp.where(keep_rows[:, None], matrix, matrix - change)
    first_cols = jnp.where(col_id == 0, lower_t.T, stepped[:, :B])
    return jnp.concatenate([first_cols, stepped[:, B:]], axis=1)


def solution(mesh):
    placed = (P("row", "col"),)
    return jax.shard_map(
        shards, mesh=mesh, in_specs=placed, out_specs=P("row", "col"), check_vma=False
    )
```

```python
import jax
import jax.numpy as jnp
from jax import lax
from jax.sharding import PartitionSpec as P

B = 64
RADIX = 2


def tree_broadcast(x, axes, size, index_of, member, radix=RADIX, have=1):
    while have < size:
        fresh = x
        for c in range(1, radix):
            lo = c * have
            if lo >= size:
                break
            pairs = []
            for src in index_of(None):
                for m in range(have):
                    if m + lo < size:
                        pairs.append((src(m), src(m + lo)))
            got = lax.ppermute(x, axes, pairs)
            take = jnp.logical_and(member >= lo, member < lo + have)
            fresh = jnp.where(take, got, fresh)
        x = fresh
        have *= radix
    return x


def shards(matrix):
    rows_dev, cols_dev = matrix.shape
    n_row = lax.axis_size("row")
    n_col = lax.axis_size("col")
    row_id = lax.axis_index("row")
    col_id = lax.axis_index("col")
    n_src = n_row // n_col
    window_cols = cols_dev * n_col // n_row

    panel_t = matrix[:, :B].T
    head = panel_t[:, :window_cols]

    def col0_group(_):
        return [lambda m: m * n_col]

    corner_t = tree_broadcast(panel_t[:, :B], ("row", "col"), n_row, col0_group, row_id, radix=8)

    bits = n_col.bit_length() - 1

    def spread(m):
        out = m & 1
        for b in range(1, bits):
            out = out | (((m >> b) & 1) << (bits - b))
        return out

    def col_groups(_):
        return [lambda m, r=r: r * n_col + spread(m) for r in range(n_row)]

    col_member = spread(col_id)

    panel_t = tree_broadcast(panel_t, ("row", "col"), 2, col_groups, col_member, radix=2, have=1)

    rel = (row_id - col_id) % n_row
    my_j = rel // n_col
    is_src = rel % n_col == 0
    corner = (corner_t + corner_t.T) / 2.0
    factor = jnp.linalg.cholesky(corner)
    inverse = lax.linalg.triangular_solve(
        factor, jnp.eye(B, dtype=factor.dtype), left_side=True, lower=True
    )
    first = jnp.concatenate([head, factor.T, inverse], axis=1)
    pieces = []
    for c in range(n_src):
        pairs = []
        for r in range(n_row):
            q = r % n_col
            if c or q:
                pairs.append((r * n_col, ((r + n_col * c) % n_row) * n_col + q))
        got = lax.ppermute(first, ("row", "col"), pairs)
        if c == 0:
            got = jnp.where(col_id == 0, first, got)
        pieces.append(got)
    panel_t, pieces = lax.optimization_barrier((panel_t, pieces))
    panel_t = tree_broadcast(panel_t, ("row", "col"), n_col // 2, col_groups, col_member, radix=2, have=2)
    fpack = pieces[0][:, window_cols:]
    pieces = [p[:, :window_cols] for p in pieces]
    ordered = []
    for jj in range(n_src):
        pick = pieces[0]
        for c in range(1, n_src):
            pick = jnp.where((my_j - jj) % n_src == c, pieces[c], pick)
        ordered.append(pick)
    packet = jnp.concatenate(ordered + [fpack], axis=1)
    packet = jnp.where(is_src, packet, jnp.zeros_like(packet))

    def row_groups(_):
        out = []
        for q in range(n_col):
            for j in range(n_src):
                base = q + n_col * j
                out.append(lambda m, base=base, q=q: ((base + m) % n_row) * n_col + q)
        return out

    packet = tree_broadcast(packet, ("row", "col"), n_col, row_groups, rel % n_col, radix=8)
    panel_t = tree_broadcast(panel_t, ("row", "col"), n_col, col_groups, col_member, radix=2, have=n_col // 2)
    panel_t, packet = lax.optimization_barrier((panel_t, packet))
    factor_t = packet[:, n_src * window_cols: n_src * window_cols + B]
    inverse = packet[:, n_src * window_cols + B:]

    tiles = []
    for k in range(cols_dev // B):
        j = k % n_src
        lt = k // n_src
        tiles.append(packet[:, j * window_cols + lt * B: j * window_cols + (lt + 1) * B])
    window_t = jnp.concatenate(tiles, axis=1)

    def apply(x):
        return lax.dot(inverse, x, precision=lax.Precision.HIGHEST,
                       preferred_element_type=jnp.float32)

    col_t = apply(window_t)
    col_t = jnp.concatenate(
        [jnp.where(col_id == 0, factor_t, col_t[:, :B]), col_t[:, B:]], axis=1
    )
    lower_t = apply(panel_t)
    lower_t = jnp.concatenate(
        [jnp.where(row_id == 0, factor_t, lower_t[:, :B]), lower_t[:, B:]], axis=1
    )
    change = lax.dot_general(
        lower_t,
        col_t,
        (((0,), (0,)), ((), ())),
        precision=lax.Precision.HIGHEST,
        preferred_element_type=jnp.float32,
    )
    local_rows = jnp.arange(rows_dev, dtype=jnp.int32)
    keep_rows = jnp.logical_and(row_id == 0, local_rows < B)
    stepped = jnp.where(keep_rows[:, None], matrix, matrix - change)
    first_cols = jnp.where(col_id == 0, lower_t.T, stepped[:, :B])
    return jnp.concatenate([first_cols, stepped[:, B:]], axis=1)


def solution(mesh):
    placed = (P("row", "col"),)
    return jax.shard_map(
        shards, mesh=mesh, in_specs=placed, out_specs=P("row", "col"), check_vma=False
    )
```
